256 devices in a mesh: tm: 16 (over y, x), space: 16 (over z, core).
Axes of the slice: x: 4, y: 4, z: 8, core: 2. Of those that a mesh axis runs over, the one named last changes fastest.
Arguments:
- query_heads: bfloat16 [32, 64, 64, 2240], P('tm', 'space'), may hold values from -10.5 to 10.5
- key_heads: bfloat16 [32, 64, 64, 2240], P('tm', 'space'), may hold values from -10.5 to 10.5
- value_heads: bfloat16 [32, 64, 64, 2240], P('tm', 'space'), may hold values from -12 to 12
- head_gain: float32 [2240], replicated, may hold values from 0.1 to 1.9
- spatial_kernel: float32 [9, 2240], replicated, may hold values from -2 to 2
- temporal_kernel: float32 [3, 2240], replicated, may hold values from -3.5 to 3.5
- out_weight: bfloat16 [2240, 2240], P('space', 'tm'), may hold values from -0.125 to 0.125
Outputs:
- mixed_out: bfloat16 [32, 64, 64, 2240], P('tm', 'space')
The draws below stay inside these ranges and needn't reach their ends.
All inputs are finite; a program needn't handle non-finite values.
Results may differ from the reference program's by a relative error of at most 0.0057.
Values may be sent and summed in bfloat16 or wider, within the bound.
No kernel may reach another device: no remote copies, remote signals or barrier semaphores. Data moves between devices by JAX's collectives and lax.ppermute only.
A program may use at most 128 MiB of HBM per device.

```python
import math
import jax
import jax.numpy as jnp
from jax import lax

HEADS = 20
HEAD_DIM = 112
D = 2240
FR = 2
WID = 64
FRAMES = 32
HEIGHT = 64
N_TM = 16


def base_values(base_key, full_shape):
    return jnp.clip(jax.random.normal(base_key, full_shape, jnp.float32), -3.5, 3.5)


def token_scaled(key, salt):
    folded = jax.random.fold_in(key, salt)
    base_key, scale_key = jax.random.split(folded)
    full_shape = (FRAMES, HEIGHT, WID, D)
    row_scale = jnp.exp(jax.random.uniform(scale_key, (FRAMES, HEIGHT, WID, 1), jnp.float32, 0.0, math.log(10.0)))
    return (0.3 * base_values(base_key, full_shape) * row_scale).astype(jnp.bfloat16)


def draw_query_heads(key, part):
    return token_scaled(key, 11)


def draw_key_heads(key, part):
    return token_scaled(key, 12)


def draw_value_heads(key, part):
    folded = jax.random.fold_in(key, 13)
    base_key, scale_key = jax.random.split(folded, 2)
    full_shape = (FRAMES, HEIGHT, WID, D)
    col_scale = jnp.exp(jax.random.uniform(scale_key, (D,), jnp.float32, 0.0, math.log(10.0)))
    values = base_values(base_key, full_shape)
    return (0.3 * values * col_scale).astype(jnp.bfloat16)


def block_scale(rng, extent, cuts, least, high):
    def one(position, blocks):
        draws = jax.random.uniform(jax.random.fold_in(jax.random.fold_in(rng, 6), position), (blocks,), jnp.float32, least / len(cuts), high / len(cuts))
        return jnp.repeat(jnp.exp(draws), extent[position] // blocks).reshape((-1,) + (1,) * (len(extent) - position - 1))

    factor_of = one(*cuts[0])
    for cut in cuts[1:]:
        factor_of = factor_of * one(*cut)
    return factor_of


def bell_draw(rng, shape, spread, reach, cuts=(), held_as=jnp.bfloat16):
    drawn = jax.random.normal(rng, shape, jnp.float32) * spread
    if len(cuts) > 0:
        drawn = block_scale(rng, shape, cuts, -0.22, 0.18) * drawn
    return jnp.clip(drawn, min=-reach, max=reach).astype(held_as)


def setup_inputs(seed: int = 0) -> dict:
    streams_of = jax.random.split(jax.random.key(seed), 8)
    query_heads = draw_query_heads(jax.random.fold_in(streams_of[7], 71), 0)
    key_heads = draw_key_heads(jax.random.fold_in(streams_of[7], 71), 0)
    value_heads = draw_value_heads(jax.random.fold_in(streams_of[7], 71), 0)
    head_gain = jnp.clip(1.0 + 0.18 * jax.random.normal(streams_of[3], (D,), jnp.float32), 0.1, 1.9)
    spatial_kernel = bell_draw(streams_of[4], (9, D), 9 ** -0.5, 2.0, (), jnp.float32)
    temporal_kernel = bell_draw(streams_of[5], (3, D), 3 ** -0.5, 3.5, (), jnp.float32)
    out_weight = bell_draw(streams_of[6], (D, D), D ** -0.5, 0.125, ((0, 16), (1, 16)))
    return dict(query_heads=query_heads, key_heads=key_heads, value_heads=value_heads, head_gain=head_gain, spatial_kernel=spatial_kernel, temporal_kernel=temporal_kernel, out_weight=out_weight)


epsilon = 1e-06

def spatial_frame(frame, spatial_kernel):
    row_count, col_count = (frame.shape[0], frame.shape[1])
    padded = jnp.pad(frame, ((1, 1), (1, 1), (0, 0)))
    summed = jnp.zeros(frame.shape, jnp.float32)
    for row_step in range(3):
        for col_step in range(3):
            summed = summed + spatial_kernel[3 * row_step + col_step] * padded[row_step:row_step + row_count, col_step:col_step + col_count].astype(jnp.float32)
    return summed.astype(jnp.bfloat16)

def reference(query_heads, key_heads, value_heads, head_gain, spatial_kernel, temporal_kernel, out_weight):
    per_block = FR * HEIGHT * WID
    block_ids = jnp.arange(N_TM, dtype=jnp.int32)

    def block_state(block_index):
        key_block = lax.dynamic_slice_in_dim(key_heads, block_index * FR, FR, 0).reshape(per_block, HEADS, HEAD_DIM)
        value_block = lax.dynamic_slice_in_dim(value_heads, block_index * FR, FR, 0).reshape(per_block, HEADS, HEAD_DIM)
        return jnp.einsum('thd,the->hde', jnp.maximum(key_block, 0).astype(jnp.float32), value_block.astype(jnp.float32))
    states = lax.map(block_state, block_ids)
    state_low = jnp.cumsum(states, axis=0).astype(jnp.bfloat16)
    spatial = lax.map(lambda frame: spatial_frame(frame, spatial_kernel), value_heads)
    padded = jnp.concatenate([jnp.zeros((2, HEIGHT, WID, D), jnp.bfloat16), spatial], axis=0)

    def block_output(block_index):
        query_block = lax.dynamic_slice_in_dim(query_heads, block_index * FR, FR, 0).reshape(per_block, HEADS, HEAD_DIM)
        attended = jnp.einsum('thd,hde->the', jnp.maximum(query_block, 0).astype(jnp.float32), state_low[block_index].astype(jnp.float32))
        mean_square = lax.optimization_barrier(jnp.mean(attended * attended, axis=-1, keepdims=True))
        normed = (attended * lax.rsqrt(mean_square + epsilon)).reshape(FR, HEIGHT, WID, D) * head_gain
        window = lax.dynamic_slice_in_dim(padded, block_index * FR, FR + 2, 0)
        temporal = jnp.zeros(normed.shape, jnp.float32)
        for back_step in range(3):
            temporal = temporal + temporal_kernel[back_step] * window[2 - back_step:2 - back_step + FR].astype(jnp.float32)
        mixed = (normed + temporal).astype(jnp.bfloat16).reshape(per_block, D)
        projected = jnp.dot(mixed, out_weight, preferred_element_type=jnp.float32)
        return projected.astype(jnp.bfloat16).reshape(FR, HEIGHT, WID, D)
    return lax.map(block_output, block_ids).reshape(FR * N_TM, HEIGHT, WID, D)
```

```python
import jax
import jax.numpy as jnp
from jax import lax
from jax.sharding import PartitionSpec as P

HEADS = 20
HEAD_DIM = 112


epsilon = 1e-06


def extended(block, sides, width):
    for axis, dim in sides:
        count = lax.axis_size(axis)
        forward = [(i, i + 1) for i in range(count - 1)]
        backward = [(target, source) for source, target in forward]
        low = lax.ppermute(
            lax.slice_in_dim(block, block.shape[dim] - width, None, axis=dim), axis, forward
        )
        high = lax.ppermute(lax.slice_in_dim(block, 0, width, axis=dim), axis, backward)
        block = jnp.concatenate([low, block, high], axis=dim)
    return block


def from_behind(block, axis, distance):
    devices = range(lax.axis_size(axis))
    route = [(i - distance, i) for i in devices if i - distance in devices]
    return lax.ppermute(block, axis, route)


def prefix_state(local_state):
    axes = ("tm", "space")
    blocks, bands = lax.axis_size("tm"), lax.axis_size("space")
    devices = blocks * bands
    flat = local_state.reshape(devices, -1)
    chunk = flat.shape[1]
    mine = lax.all_to_all(flat, axes, 0, 0, tiled=True)
    block_sums = mine.reshape(blocks, bands, chunk).sum(axis=1)
    prefixes = jnp.cumsum(block_sums, axis=0).astype(jnp.bfloat16)
    outgoing = jnp.broadcast_to(prefixes[:, None, :], (blocks, bands, chunk)).reshape(devices, chunk)
    gathered = lax.all_to_all(outgoing, axes, 0, 0, tiled=True)
    return gathered.reshape(local_state.shape)


def spatial_conv(padded, spatial_kernel):
    frame_count = padded.shape[0]
    row_count = padded.shape[1] - 2
    col_count = padded.shape[2]
    widened = jnp.pad(padded, ((0, 0), (0, 0), (1, 1), (0, 0)))
    summed = jnp.zeros((frame_count, row_count, col_count, padded.shape[3]), jnp.float32)
    for row_step in range(3):
        for col_step in range(3):
            summed = summed + spatial_kernel[3 * row_step + col_step] * widened[
                :, row_step : row_step + row_count, col_step : col_step + col_count
            ].astype(jnp.float32)
    return summed.astype(jnp.bfloat16)


def per_device(
    query_heads, key_heads, value_heads, head_gain, spatial_kernel, temporal_kernel, out_weight
):
    frame_count, row_count, col_count, model_width = query_heads.shape
    weight_band = lax.all_gather(out_weight, "tm", axis=1, tiled=True)
    weight_stack = lax.all_gather(weight_band, "space", axis=0)
    token_count = frame_count * row_count * col_count
    queries = query_heads.reshape(token_count, HEADS, HEAD_DIM)
    key_rows = key_heads.reshape(token_count, HEADS, HEAD_DIM)
    value_rows = value_heads.reshape(token_count, HEADS, HEAD_DIM)
    local_state = jnp.einsum(
        "thd,the->hde", jnp.maximum(key_rows, 0), value_rows, preferred_element_type=jnp.float32
    )
    state_low = prefix_state(local_state)
    attended = jnp.einsum(
        "thd,hde->the", jnp.maximum(queries, 0), state_low, preferred_element_type=jnp.float32
    )
    mean_square = jnp.mean(attended * attended, axis=-1, keepdims=True)
    normed = (attended * lax.rsqrt(mean_square + epsilon)).reshape(
        frame_count, row_count, col_count, model_width
    ) * head_gain
    padded = extended(value_heads, (("space", 1),), 1)
    spatial = spatial_conv(padded, spatial_kernel)
    earlier_frames = from_behind(spatial, "tm", 1)
    window = jnp.concatenate([earlier_frames, spatial], axis=0)
    temporal = jnp.zeros(normed.shape, jnp.float32)
    for back_step in range(3):
        temporal = temporal + temporal_kernel[back_step] * window[
            2 - back_step : 2 - back_step + frame_count
        ].astype(jnp.float32)
    mixed = (normed + temporal).astype(jnp.bfloat16).reshape(token_count, model_width)
    space_count = lax.axis_size("space")
    projected = jnp.einsum(
        "tsk,skc->tc",
        mixed.reshape(token_count, space_count, model_width // space_count),
        weight_stack,
        preferred_element_type=jnp.float32,
    )
    return projected.astype(jnp.bfloat16).reshape(frame_count, row_count, col_count, model_width)


def solution(mesh):
    placed = (
        P("tm", "space", None, None),
        P("tm", "space", None, None),
        P("tm", "space", None, None),
        P(),
        P(),
        P(),
        P("space", "tm"),
    )
    return jax.shard_map(
        per_device,
        mesh=mesh,
        in_specs=placed,
        out_specs=P("tm", "space", None, None),
        check_vma=False,
    )
```

```python
import math

import jax
import jax.numpy as jnp
from jax import lax
from jax.sharding import PartitionSpec as P

HEADS = 20
HEAD_DIM = 112


epsilon = 1e-06


def extended(block, sides, width):
    for axis, dim in sides:
        count = lax.axis_size(axis)
        forward = [(i, i + 1) for i in range(count - 1)]
        backward = [(target, source) for source, target in forward]
        low = lax.ppermute(
            lax.slice_in_dim(block, block.shape[dim] - width, None, axis=dim), axis, forward
        )
        high = lax.ppermute(lax.slice_in_dim(block, 0, width, axis=dim), axis, backward)
        block = jnp.concatenate([low, block, high], axis=dim)
    return block


def from_behind(block, axis, distance):
    devices = range(lax.axis_size(axis))
    route = [(i - distance, i) for i in devices if i - distance in devices]
    return lax.ppermute(block, axis, route)


def prefix_state(local_state):
    axes = ("tm", "space")
    blocks, bands = lax.axis_size("tm"), lax.axis_size("space")
    devices = blocks * bands
    flat = local_state.reshape(devices, -1)
    chunk = flat.shape[1]
    mine = lax.all_to_all(flat, axes, 0, 0, tiled=True)
    block_sums = mine.reshape(blocks, bands, chunk).sum(axis=1)
    prefixes = jnp.cumsum(block_sums, axis=0).astype(jnp.bfloat16)
    outgoing = jnp.broadcast_to(prefixes[:, None, :], (blocks, bands, chunk)).reshape(devices, chunk)
    gathered = lax.all_to_all(outgoing, axes, 0, 0, tiled=True)
    return gathered.reshape(local_state.shape)


def spatial_conv(padded, spatial_kernel):
    frame_count = padded.shape[0]
    row_count = padded.shape[1] - 2
    col_count = padded.shape[2]
    widened = jnp.pad(padded, ((0, 0), (0, 0), (1, 1), (0, 0)))
    summed = jnp.zeros((frame_count, row_count, col_count, padded.shape[3]), jnp.float32)
    for row_step in range(3):
        for col_step in range(3):
            summed = summed + spatial_kernel[3 * row_step + col_step] * widened[
                :, row_step : row_step + row_count, col_step : col_step + col_count
            ].astype(jnp.float32)
    return summed.astype(jnp.bfloat16)


def banded_attention(queries, state_low):
    heads, dim, _ = state_low.shape
    group = math.lcm(dim, 128) // dim
    pieces = []
    for first in range(0, heads, group):
        count = min(group, heads - first)
        blocks = state_low[first : first + count]
        eye = jnp.eye(count, dtype=bool)
        diagonal = jnp.where(
            eye[:, None, :, None], blocks[:, :, None, :], jnp.zeros((), blocks.dtype)
        ).reshape(count * dim, count * dim)
        pieces.append(
            jnp.dot(
                queries[:, first * dim : (first + count) * dim],
                diagonal,
                preferred_element_type=jnp.float32,
            )
        )
    return jnp.concatenate(pieces, axis=1)


def split_dot(values, matrix):
    high = values.astype(jnp.bfloat16)
    low = (values - high.astype(jnp.float32)).astype(jnp.bfloat16)
    return jnp.dot(high, matrix, preferred_element_type=jnp.float32) + jnp.dot(
        low, matrix, preferred_element_type=jnp.float32
    )


def head_norm(attended):
    width = attended.shape[1]
    member = (jnp.arange(width)[:, None] // HEAD_DIM == jnp.arange(HEADS)[None, :]).astype(jnp.bfloat16)
    mean_square = split_dot(attended * attended, member) / HEAD_DIM
    scale = split_dot(lax.rsqrt(mean_square + epsilon), member.T)
    return attended * scale


def per_device(
    query_heads, key_heads, value_heads, head_gain, spatial_kernel, temporal_kernel, out_weight
):
    frame_count, row_count, col_count, model_width = query_heads.shape
    weight_band = lax.all_gather(out_weight, "tm", axis=1, tiled=True)
    weight_stack = lax.all_gather(weight_band, "space", axis=0)
    token_count = frame_count * row_count * col_count
    queries = query_heads.reshape(token_count, HEADS, HEAD_DIM)
    key_rows = key_heads.reshape(token_count, HEADS, HEAD_DIM)
    value_rows = value_heads.reshape(token_count, HEADS, HEAD_DIM)
    local_state = jnp.einsum(
        "thd,the->hde", jnp.maximum(key_rows, 0), value_rows, preferred_element_type=jnp.float32
    )
    state_low = prefix_state(local_state)
    flat_queries = jnp.maximum(query_heads.reshape(token_count, model_width), 0)
    attended = banded_attention(flat_queries, state_low)
    normed = head_norm(attended).reshape(frame_count, row_count, col_count, model_width) * head_gain
    padded = extended(value_heads, (("space", 1),), 1)
    spatial = spatial_conv(padded, spatial_kernel)
    earlier_frames = from_behind(spatial, "tm", 1)
    window = jnp.concatenate([earlier_frames, spatial], axis=0)
    temporal = jnp.zeros(normed.shape, jnp.float32)
    for back_step in range(3):
        temporal = temporal + temporal_kernel[back_step] * window[
            2 - back_step : 2 - back_step + frame_count
        ].astype(jnp.float32)
    mixed = (normed + temporal).astype(jnp.bfloat16).reshape(token_count, model_width)
    projected = jnp.dot(
        mixed, weight_stack.reshape(model_width, model_width), preferred_element_type=jnp.float32
    )
    return projected.astype(jnp.bfloat16).reshape(frame_count, row_count, col_count, model_width)


def solution(mesh):
    placed = (
        P("tm", "space", None, None),
        P("tm", "space", None, None),
        P("tm", "space", None, None),
        P(),
        P(),
        P(),
        P("space", "tm"),
    )
    return jax.shard_map(
        per_device,
        mesh=mesh,
        in_specs=placed,
        out_specs=P("tm", "space", None, None),
        check_vma=False,
    )
```

```python
import math

import jax
import jax.numpy as jnp
from jax import lax
from jax.sharding import PartitionSpec as P

HEADS = 20
HEAD_DIM = 112


epsilon = 1e-06


def extended(block, sides, width):
    for axis, dim in sides:
        count = lax.axis_size(axis)
        forward = [(i, i + 1) for i in range(count - 1)]
        backward = [(target, source) for source, target in forward]
        low = lax.ppermute(
            lax.slice_in_dim(block, block.shape[dim] - width, None, axis=dim), axis, forward
        )
        high = lax.ppermute(lax.slice_in_dim(block, 0, width, axis=dim), axis, backward)
        block = jnp.concatenate([low, block, high], axis=dim)
    return block


def from_behind(block, axis, distance):
    devices = range(lax.axis_size(axis))
    route = [(i - distance, i) for i in devices if i - distance in devices]
    return lax.ppermute(block, axis, route)


def prefix_state(local_state, beside_out, beside_back):
    axes = ("tm", "space")
    blocks, bands = lax.axis_size("tm"), lax.axis_size("space")
    devices = blocks * bands
    flat = local_state.reshape(devices, -1)
    chunk = flat.shape[1]
    mine = lax.all_to_all(flat, axes, 0, 0, tiled=True)
    mine, beside_out = lax.optimization_barrier((mine, beside_out))
    block_sums = mine.reshape(blocks, bands, chunk).sum(axis=1)
    prefixes = jnp.cumsum(block_sums, axis=0).astype(jnp.bfloat16)
    outgoing = jnp.broadcast_to(prefixes[:, None, :], (blocks, bands, chunk)).reshape(devices, chunk)
    gathered = lax.all_to_all(outgoing, axes, 0, 0, tiled=True)
    gathered, beside_back = lax.optimization_barrier((gathered, beside_back))
    return gathered.reshape(local_state.shape), beside_out, beside_back


def spatial_conv(padded, spatial_kernel):
    frame_count = padded.shape[0]
    row_count = padded.shape[1] - 2
    col_count = padded.shape[2]
    widened = jnp.pad(padded, ((0, 0), (0, 0), (1, 1), (0, 0)))
    summed = jnp.zeros((frame_count, row_count, col_count, padded.shape[3]), jnp.float32)
    for row_step in range(3):
        for col_step in range(3):
            summed = summed + spatial_kernel[3 * row_step + col_step] * widened[
                :, row_step : row_step + row_count, col_step : col_step + col_count
            ].astype(jnp.float32)
    return summed.astype(jnp.bfloat16)


def banded_attention(queries, state_low):
    heads, dim, _ = state_low.shape
    group = math.lcm(dim, 128) // dim
    pieces = []
    for first in range(0, heads, group):
        count = min(group, heads - first)
        blocks = state_low[first : first + count]
        eye = jnp.eye(count, dtype=bool)
        diagonal = jnp.where(
            eye[:, None, :, None], blocks[:, :, None, :], jnp.zeros((), blocks.dtype)
        ).reshape(count * dim, count * dim)
        pieces.append(
            jnp.dot(
                queries[:, first * dim : (first + count) * dim],
                diagonal,
                preferred_element_type=jnp.float32,
            )
        )
    return jnp.concatenate(pieces, axis=1)


def split_dot(values, matrix):
    high = lax.reduce_precision(values, exponent_bits=8, mantissa_bits=7)
    low = values - high
    return jnp.dot(
        high.astype(jnp.bfloat16), matrix, preferred_element_type=jnp.float32
    ) + jnp.dot(low.astype(jnp.bfloat16), matrix, preferred_element_type=jnp.float32)


def head_norm(attended):
    width = attended.shape[1]
    member = (jnp.arange(width)[:, None] // HEAD_DIM == jnp.arange(HEADS)[None, :]).astype(jnp.bfloat16)
    mean_square = split_dot(attended * attended, member) / HEAD_DIM
    scale = split_dot(lax.rsqrt(mean_square + epsilon), member.T)
    return attended * scale


def per_device(
    query_heads, key_heads, value_heads, head_gain, spatial_kernel, temporal_kernel, out_weight
):
    frame_count, row_count, col_count, model_width = query_heads.shape
    weight_band = lax.all_gather(out_weight, "tm", axis=1, tiled=True)
    weight_stack = lax.all_gather(weight_band, "space", axis=0)
    token_count = frame_count * row_count * col_count
    queries = query_heads.reshape(token_count, HEADS, HEAD_DIM)
    key_rows = key_heads.reshape(token_count, HEADS, HEAD_DIM)
    value_rows = value_heads.reshape(token_count, HEADS, HEAD_DIM)
    local_state = jnp.einsum(
        "thd,the->hde", jnp.maximum(key_rows, 0), value_rows, preferred_element_type=jnp.float32
    )
    padded = extended(value_heads, (("space", 1),), 1)
    spatial = spatial_conv(padded, spatial_kernel)
    earlier_frames = from_behind(spatial, "tm", 1)
    weight_flat = weight_stack.reshape(model_width, model_width)
    state_low, spatial, weight_flat = prefix_state(local_state, spatial, weight_flat)
    flat_queries = jnp.maximum(query_heads.reshape(token_count, model_width), 0)
    attended = banded_attention(flat_queries, state_low)
    normed = head_norm(attended).reshape(frame_count, row_count, col_count, model_width) * head_gain
    window = jnp.concatenate([earlier_frames, spatial], axis=0)
    temporal = jnp.zeros(normed.shape, jnp.float32)
    for back_step in range(3):
        temporal = temporal + temporal_kernel[back_step] * window[
            2 - back_step : 2 - back_step + frame_count
        ].astype(jnp.float32)
    mixed = (normed + temporal).astype(jnp.bfloat16).reshape(token_count, model_width)
    projected = jnp.dot(
        mixed, weight_flat, preferred_element_type=jnp.float32
    )
    return projected.astype(jnp.bfloat16).reshape(frame_count, row_count, col_count, model_width)


def solution(mesh):
    placed = (
        P("tm", "space", None, None),
        P("tm", "space", None, None),
        P("tm", "space", None, None),
        P(),
        P(),
        P(),
        P("space", "tm"),
    )
    return jax.shard_map(
        per_device,
        mesh=mesh,
        in_specs=placed,
        out_specs=P("tm", "space", None, None),
        check_vma=False,
    )
```

```python
import math

import jax
import jax.numpy as jnp
from jax import lax
from jax.sharding import PartitionSpec as P

HEADS = 20
HEAD_DIM = 112


epsilon = 1e-06


def extended(block, sides, width):
    for axis, dim in sides:
        count = lax.axis_size(axis)
        forward = [(i, i + 1) for i in range(count - 1)]
        backward = [(target, source) for source, target in forward]
        low = lax.ppermute(
            lax.slice_in_dim(block, block.shape[dim] - width, None, axis=dim), axis, forward
        )
        high = lax.ppermute(lax.slice_in_dim(block, 0, width, axis=dim), axis, backward)
        block = jnp.concatenate([low, block, high], axis=dim)
    return block


def from_behind(block, axis, distance):
    devices = range(lax.axis_size(axis))
    route = [(i - distance, i) for i in devices if i - distance in devices]
    return lax.ppermute(block, axis, route)


def prefix_state(local_state, beside_out, beside_back):
    axes = ("tm", "space")
    blocks, bands = lax.axis_size("tm"), lax.axis_size("space")
    devices = blocks * bands
    flat = local_state.reshape(devices, -1)
    chunk = flat.shape[1]
    mine = lax.all_to_all(flat, axes, 0, 0, tiled=True)
    mine, beside_out = lax.optimization_barrier((mine, beside_out))
    block_sums = mine.reshape(blocks, bands, chunk).sum(axis=1)
    prefixes = jnp.cumsum(block_sums, axis=0).astype(jnp.bfloat16)
    outgoing = jnp.broadcast_to(prefixes[:, None, :], (blocks, bands, chunk)).reshape(devices, chunk)
    gathered = lax.all_to_all(outgoing, axes, 0, 0, tiled=True)
    gathered, beside_back = lax.optimization_barrier((gathered, beside_back))
    return gathered.reshape(local_state.shape), beside_out, beside_back


def spatial_conv(padded, spatial_kernel):
    frame_count = padded.shape[0]
    row_count = padded.shape[1] - 2
    col_count = padded.shape[2]
    widened = jnp.pad(padded, ((0, 0), (0, 0), (1, 1), (0, 0)))
    summed = jnp.zeros((frame_count, row_count, col_count, padded.shape[3]), jnp.float32)
    for row_step in range(3):
        for col_step in range(3):
            summed = summed + spatial_kernel[3 * row_step + col_step] * widened[
                :, row_step : row_step + row_count, col_step : col_step + col_count
            ].astype(jnp.float32)
    return summed.astype(jnp.bfloat16)


def banded_attention(queries, state_low):
    heads, dim, _ = state_low.shape
    group = math.lcm(dim, 128) // dim
    pieces = []
    for first in range(0, heads, group):
        count = min(group, heads - first)
        blocks = state_low[first : first + count]
        eye = jnp.eye(count, dtype=bool)
        diagonal = jnp.where(
            eye[:, None, :, None], blocks[:, :, None, :], jnp.zeros((), blocks.dtype)
        ).reshape(count * dim, count * dim)
        pieces.append(
            jnp.dot(
                queries[:, first * dim : (first + count) * dim],
                diagonal,
                preferred_element_type=jnp.float32,
            )
        )
    return jnp.concatenate(pieces, axis=1)


def split_dot(values, matrix):
    high = lax.reduce_precision(values, exponent_bits=8, mantissa_bits=7)
    low = values - high
    return jnp.dot(
        high.astype(jnp.bfloat16), matrix, preferred_element_type=jnp.float32
    ) + jnp.dot(low.astype(jnp.bfloat16), matrix, preferred_element_type=jnp.float32)


def head_norm(attended):
    width = attended.shape[1]
    member = (jnp.arange(width)[:, None] // HEAD_DIM == jnp.arange(HEADS)[None, :]).astype(jnp.bfloat16)
    mean_square = split_dot(attended * attended, member) / HEAD_DIM
    scale = split_dot(lax.rsqrt(mean_square + epsilon), member.T)
    return attended * scale


def per_device(
    query_heads, key_heads, value_heads, head_gain, spatial_kernel, temporal_kernel, out_weight
):
    frame_count, row_count, col_count, model_width = query_heads.shape
    weight_cols = lax.all_gather(out_weight, "space", axis=0, tiled=True)
    weight_stack = lax.all_gather(weight_cols, "tm", axis=0)
    token_count = frame_count * row_count * col_count
    queries = query_heads.reshape(token_count, HEADS, HEAD_DIM)
    key_rows = key_heads.reshape(token_count, HEADS, HEAD_DIM)
    value_rows = value_heads.reshape(token_count, HEADS, HEAD_DIM)
    local_state = jnp.einsum(
        "thd,the->hde", jnp.maximum(key_rows, 0), value_rows, preferred_element_type=jnp.float32
    )
    padded = extended(value_heads, (("space", 1),), 1)
    spatial = spatial_conv(padded, spatial_kernel)
    earlier_frames = from_behind(spatial, "tm", 1)
    weight_flat = weight_stack.transpose(1, 0, 2).reshape(model_width, model_width)
    state_low, spatial, weight_flat = prefix_state(local_state, spatial, weight_flat)
    flat_queries = jnp.maximum(query_heads.reshape(token_count, model_width), 0)
    attended = banded_attention(flat_queries, state_low)
    normed = head_norm(attended).reshape(frame_count, row_count, col_count, model_width) * head_gain
    window = jnp.concatenate([earlier_frames, spatial], axis=0)
    temporal = jnp.zeros(normed.shape, jnp.float32)
    for back_step in range(3):
        temporal = temporal + temporal_kernel[back_step] * window[
            2 - back_step : 2 - back_step + frame_count
        ].astype(jnp.float32)
    mixed = (normed + temporal).astype(jnp.bfloat16).reshape(token_count, model_width)
    projected = jnp.dot(
        mixed, weight_flat, preferred_element_type=jnp.float32
    )
    return projected.astype(jnp.bfloat16).reshape(frame_count, row_count, col_count, model_width)


def solution(mesh):
    placed = (
        P("tm", "space", None, None),
        P("tm", "space", None, None),
        P("tm", "space", None, None),
        P(),
        P(),
        P(),
        P("space", "tm"),
    )
    return jax.shard_map(
        per_device,
        mesh=mesh,
        in_specs=placed,
        out_specs=P("tm", "space", None, None),
        check_vma=False,
    )
```

```python
import math

import jax
import jax.numpy as jnp
from jax import lax
from jax.sharding import PartitionSpec as P

HEADS = 20
HEAD_DIM = 112


epsilon = 1e-06


def extended(block, sides, width):
    for axis, dim in sides:
        count = lax.axis_size(axis)
        forward = [(i, i + 1) for i in range(count - 1)]
        backward = [(target, source) for source, target in forward]
        low = lax.ppermute(
            lax.slice_in_dim(block, block.shape[dim] - width, None, axis=dim), axis, forward
        )
        high = lax.ppermute(lax.slice_in_dim(block, 0, width, axis=dim), axis, backward)
        block = jnp.concatenate([low, block, high], axis=dim)
    return block


def from_behind(block, axis, distance):
    devices = range(lax.axis_size(axis))
    route = [(i - distance, i) for i in devices if i - distance in devices]
    return lax.ppermute(block, axis, route)


def prefix_state(local_state, beside_out, beside_back):
    axes = ("tm", "space")
    blocks, bands = lax.axis_size("tm"), lax.axis_size("space")
    devices = blocks * bands
    flat = local_state.reshape(devices, -1)
    chunk = flat.shape[1]
    mine = lax.all_to_all(flat, axes, 0, 0, tiled=True)
    mine, beside_out = lax.optimization_barrier((mine, beside_out))
    block_sums = mine.reshape(blocks, bands, chunk).sum(axis=1)
    prefixes = jnp.cumsum(block_sums, axis=0).astype(jnp.bfloat16)
    outgoing = jnp.broadcast_to(prefixes[:, None, :], (blocks, bands, chunk)).reshape(devices, chunk)
    gathered = lax.all_to_all(outgoing, axes, 0, 0, tiled=True)
    gathered, beside_back = lax.optimization_barrier((gathered, beside_back))
    return gathered.reshape(local_state.shape), beside_out, beside_back


def spatial_conv(padded, spatial_kernel):
    frame_count = padded.shape[0]
    row_count = padded.shape[1] - 2
    col_count = padded.shape[2]
    widened = jnp.pad(padded, ((0, 0), (0, 0), (1, 1), (0, 0)))
    summed = jnp.zeros((frame_count, row_count, col_count, padded.shape[3]), jnp.float32)
    for row_step in range(3):
        for col_step in range(3):
            summed = summed + spatial_kernel[3 * row_step + col_step] * widened[
                :, row_step : row_step + row_count, col_step : col_step + col_count
            ].astype(jnp.float32)
    return summed.astype(jnp.bfloat16)


def banded_attention(queries, state_low):
    heads, dim, _ = state_low.shape
    group = math.lcm(dim, 128) // dim
    pieces = []
    for first in range(0, heads, group):
        count = min(group, heads - first)
        blocks = state_low[first : first + count]
        eye = jnp.eye(count, dtype=bool)
        diagonal = jnp.where(
            eye[:, None, :, None], blocks[:, :, None, :], jnp.zeros((), blocks.dtype)
        ).reshape(count * dim, count * dim)
        pieces.append(
            jnp.dot(
                queries[:, first * dim : (first + count) * dim],
                diagonal,
                preferred_element_type=jnp.float32,
            )
        )
    return jnp.concatenate(pieces, axis=1)


def split_dot(values, matrix):
    high = lax.reduce_precision(values, exponent_bits=8, mantissa_bits=7)
    low = values - high
    return jnp.dot(
        high.astype(jnp.bfloat16), matrix, preferred_element_type=jnp.float32
    ) + jnp.dot(low.astype(jnp.bfloat16), matrix, preferred_element_type=jnp.float32)


def head_norm(attended):
    width = attended.shape[1]
    member = (jnp.arange(width)[:, None] // HEAD_DIM == jnp.arange(HEADS)[None, :]).astype(jnp.bfloat16)
    mean_square = split_dot(attended * attended, member) / HEAD_DIM
    scale = split_dot(lax.rsqrt(mean_square + epsilon), member.T)
    return attended * scale


def per_device(
    query_heads, key_heads, value_heads, head_gain, spatial_kernel, temporal_kernel, out_weight
):
    frame_count, row_count, col_count, model_width = query_heads.shape
    weight_cols = lax.all_gather(out_weight, "space", axis=0, tiled=True)
    column_pad = -weight_cols.shape[1] % 16
    weight_stack = lax.all_gather(jnp.pad(weight_cols, ((0, 0), (0, column_pad))), "tm", axis=0)
    token_count = frame_count * row_count * col_count
    queries = query_heads.reshape(token_count, HEADS, HEAD_DIM)
    key_rows = key_heads.reshape(token_count, HEADS, HEAD_DIM)
    value_rows = value_heads.reshape(token_count, HEADS, HEAD_DIM)
    local_state = jnp.einsum(
        "thd,the->hde", jnp.maximum(key_rows, 0), value_rows, preferred_element_type=jnp.float32
    )
    padded = extended(value_heads, (("space", 1),), 1)
    spatial = spatial_conv(padded, spatial_kernel)
    earlier_frames = from_behind(spatial, "tm", 1)
    blocks, _, padded_width = weight_stack.shape
    weight_flat = weight_stack.transpose(1, 0, 2).reshape(model_width, blocks * padded_width)
    state_low, spatial, weight_flat = prefix_state(local_state, spatial, weight_flat)
    flat_queries = jnp.maximum(query_heads.reshape(token_count, model_width), 0)
    attended = banded_attention(flat_queries, state_low)
    normed = head_norm(attended).reshape(frame_count, row_count, col_count, model_width) * head_gain
    window = jnp.concatenate([earlier_frames, spatial], axis=0)
    temporal = jnp.zeros(normed.shape, jnp.float32)
    for back_step in range(3):
        temporal = temporal + temporal_kernel[back_step] * window[
            2 - back_step : 2 - back_step + frame_count
        ].astype(jnp.float32)
    mixed = (normed + temporal).astype(jnp.bfloat16).reshape(token_count, model_width)
    projected = jnp.dot(mixed, weight_flat, preferred_element_type=jnp.float32)
    projected = projected.reshape(token_count, blocks, padded_width)[:, :, : padded_width - column_pad]
    return projected.astype(jnp.bfloat16).reshape(frame_count, row_count, col_count, model_width)


def solution(mesh):
    placed = (
        P("tm", "space", None, None),
        P("tm", "space", None, None),
        P("tm", "space", None, None),
        P(),
        P(),
        P(),
        P("space", "tm"),
    )
    return jax.shard_map(
        per_device,
        mesh=mesh,
        in_specs=placed,
        out_specs=P("tm", "space", None, None),
        check_vma=False,
    )
```

```python
import math

import jax
import jax.numpy as jnp
from jax import lax
from jax.sharding import PartitionSpec as P

HEADS = 20
HEAD_DIM = 112


epsilon = 1e-06


def extended(block, sides, width):
    for axis, dim in sides:
        count = lax.axis_size(axis)
        forward = [(i, i + 1) for i in range(count - 1)]
        backward = [(target, source) for source, target in forward]
        low = lax.ppermute(
            lax.slice_in_dim(block, block.shape[dim] - width, None, axis=dim), axis, forward
        )
        high = lax.ppermute(lax.slice_in_dim(block, 0, width, axis=dim), axis, backward)
        block = jnp.concatenate([low, block, high], axis=dim)
    return block


def from_behind(block, axis, distance):
    devices = range(lax.axis_size(axis))
    route = [(i - distance, i) for i in devices if i - distance in devices]
    return lax.ppermute(block, axis, route)


def prefix_state(local_state, beside_out, beside_back):
    axes = ("tm", "space")
    blocks, bands = lax.axis_size("tm"), lax.axis_size("space")
    devices = blocks * bands
    flat = local_state.reshape(devices, -1)
    chunk = flat.shape[1]
    mine = lax.all_to_all(flat, axes, 0, 0, tiled=True)
    mine, beside_out = lax.optimization_barrier((mine, beside_out))
    block_sums = mine.reshape(blocks, bands, chunk).sum(axis=1)
    prefixes = jnp.cumsum(block_sums, axis=0).astype(jnp.bfloat16)
    outgoing = jnp.broadcast_to(prefixes[:, None, :], (blocks, bands, chunk)).reshape(devices, chunk)
    gathered = lax.all_to_all(outgoing, axes, 0, 0, tiled=True)
    gathered, beside_back = lax.optimization_barrier((gathered, beside_back))
    return gathered.reshape(local_state.shape), beside_out, beside_back


def spatial_conv(padded, spatial_kernel):
    frame_count = padded.shape[0]
    row_count = padded.shape[1] - 2
    col_count = padded.shape[2]
    widened = jnp.pad(padded, ((0, 0), (0, 0), (1, 1), (0, 0)))
    summed = jnp.zeros((frame_count, row_count, col_count, padded.shape[3]), jnp.float32)
    for row_step in range(3):
        for col_step in range(3):
            summed = summed + spatial_kernel[3 * row_step + col_step] * widened[
                :, row_step : row_step + row_count, col_step : col_step + col_count
            ].astype(jnp.float32)
    return summed.astype(jnp.bfloat16)


def banded_attention(queries, state_low):
    heads, dim, _ = state_low.shape
    group = math.lcm(dim, 128) // dim
    pieces = []
    for first in range(0, heads, group):
        count = min(group, heads - first)
        blocks = state_low[first : first + count]
        eye = jnp.eye(count, dtype=bool)
        diagonal = jnp.where(
            eye[:, None, :, None], blocks[:, :, None, :], jnp.zeros((), blocks.dtype)
        ).reshape(count * dim, count * dim)
        pieces.append(
            jnp.dot(
                queries[:, first * dim : (first + count) * dim],
                diagonal,
                preferred_element_type=jnp.float32,
            )
        )
    return jnp.concatenate(pieces, axis=1)


def split_dot(values, matrix):
    high = lax.reduce_precision(values, exponent_bits=8, mantissa_bits=7)
    low = values - high
    return jnp.dot(
        high.astype(jnp.bfloat16), matrix, preferred_element_type=jnp.float32
    ) + jnp.dot(low.astype(jnp.bfloat16), matrix, preferred_element_type=jnp.float32)


def head_norm(attended):
    width = attended.shape[1]
    member = (jnp.arange(width)[:, None] // HEAD_DIM == jnp.arange(HEADS)[None, :]).astype(jnp.bfloat16)
    mean_square = split_dot(attended * attended, member) / HEAD_DIM
    scale = split_dot(lax.rsqrt(mean_square + epsilon), member.T)
    return attended * scale


def per_device(
    query_heads, key_heads, value_heads, head_gain, spatial_kernel, temporal_kernel, out_weight
):
    frame_count, row_count, col_count, model_width = query_heads.shape
    bands = lax.axis_size("space")
    copies = jnp.broadcast_to(out_weight[None], (bands,) + out_weight.shape)
    weight_cols = lax.all_to_all(copies, "space", 0, 0, tiled=True).reshape(-1, out_weight.shape[1])
    weight_stack = lax.all_gather(weight_cols, "tm", axis=0)
    token_count = frame_count * row_count * col_count
    queries = query_heads.reshape(token_count, HEADS, HEAD_DIM)
    key_rows = key_heads.reshape(token_count, HEADS, HEAD_DIM)
    value_rows = value_heads.reshape(token_count, HEADS, HEAD_DIM)
    local_state = jnp.einsum(
        "thd,the->hde", jnp.maximum(key_rows, 0), value_rows, preferred_element_type=jnp.float32
    )
    padded = extended(value_heads, (("space", 1),), 1)
    spatial = spatial_conv(padded, spatial_kernel)
    earlier_frames = from_behind(spatial, "tm", 1)
    weight_flat = weight_stack.transpose(1, 0, 2).reshape(model_width, model_width)
    state_low, spatial, (weight_flat, earlier_frames) = prefix_state(
        local_state, spatial, (weight_flat, earlier_frames)
    )
    flat_queries = jnp.maximum(query_heads.reshape(token_count, model_width), 0)
    attended = banded_attention(flat_queries, state_low)
    normed = head_norm(attended).reshape(frame_count, row_count, col_count, model_width) * head_gain
    window = jnp.concatenate([earlier_frames, spatial], axis=0)
    temporal = jnp.zeros(normed.shape, jnp.float32)
    for back_step in range(3):
        temporal = temporal + temporal_kernel[back_step] * window[
            2 - back_step : 2 - back_step + frame_count
        ].astype(jnp.float32)
    mixed = (normed + temporal).astype(jnp.bfloat16).reshape(token_count, model_width)
    projected = jnp.dot(
        mixed, weight_flat, preferred_element_type=jnp.float32
    )
    return projected.astype(jnp.bfloat16).reshape(frame_count, row_count, col_count, model_width)


def solution(mesh):
    placed = (
        P("tm", "space", None, None),
        P("tm", "space", None, None),
        P("tm", "space", None, None),
        P(),
        P(),
        P(),
        P("space", "tm"),
    )
    return jax.shard_map(
        per_device,
        mesh=mesh,
        in_specs=placed,
        out_specs=P("tm", "space", None, None),
        check_vma=False,
    )
```

```python
import math

import jax
import jax.numpy as jnp
from jax import lax
from jax.sharding import PartitionSpec as P

HEADS = 20
HEAD_DIM = 112


epsilon = 1e-06


def extended(block, sides, width):
    for axis, dim in sides:
        count = lax.axis_size(axis)
        forward = [(i, i + 1) for i in range(count - 1)]
        backward = [(target, source) for source, target in forward]
        low = lax.ppermute(
            lax.slice_in_dim(block, block.shape[dim] - width, None, axis=dim), axis, forward
        )
        high = lax.ppermute(lax.slice_in_dim(block, 0, width, axis=dim), axis, backward)
        block = jnp.concatenate([low, block, high], axis=dim)
    return block


def from_behind(block, axis, distance):
    devices = range(lax.axis_size(axis))
    route = [(i - distance, i) for i in devices if i - distance in devices]
    return lax.ppermute(block, axis, route)


def prefix_state(local_state, beside_out, beside_back):
    axes = ("tm", "space")
    blocks, bands = lax.axis_size("tm"), lax.axis_size("space")
    devices = blocks * bands
    flat = local_state.reshape(devices, -1)
    chunk = flat.shape[1]
    mine = lax.all_to_all(flat, axes, 0, 0, tiled=True)
    mine, beside_out = lax.optimization_barrier((mine, beside_out))
    block_sums = mine.reshape(blocks, bands, chunk).sum(axis=1)
    prefixes = jnp.cumsum(block_sums, axis=0).astype(jnp.bfloat16)
    outgoing = jnp.broadcast_to(prefixes[:, None, :], (blocks, bands, chunk)).reshape(devices, chunk)
    gathered = lax.all_to_all(outgoing, axes, 0, 0, tiled=True)
    gathered, beside_back = lax.optimization_barrier((gathered, beside_back))
    return gathered.reshape(local_state.shape), beside_out, beside_back


def spatial_conv(padded, spatial_kernel):
    frame_count = padded.shape[0]
    row_count = padded.shape[1] - 2
    col_count = padded.shape[2]
    widened = jnp.pad(padded, ((0, 0), (0, 0), (1, 1), (0, 0)))
    summed = jnp.zeros((frame_count, row_count, col_count, padded.shape[3]), jnp.float32)
    for row_step in range(3):
        for col_step in range(3):
            summed = summed + spatial_kernel[3 * row_step + col_step] * widened[
                :, row_step : row_step + row_count, col_step : col_step + col_count
            ].astype(jnp.float32)
    return summed.astype(jnp.bfloat16)


def banded_attention(queries, state_low):
    heads, dim, _ = state_low.shape
    group = math.lcm(dim, 128) // dim
    pieces = []
    for first in range(0, heads, group):
        count = min(group, heads - first)
        blocks = state_low[first : first + count]
        diagonal = jnp.zeros((count * dim, count * dim), blocks.dtype)
        for head in range(count):
            diagonal = lax.dynamic_update_slice(diagonal, blocks[head], (head * dim, head * dim))
        pieces.append(
            jnp.dot(
                queries[:, first * dim : (first + count) * dim],
                diagonal,
                preferred_element_type=jnp.float32,
            )
        )
    return jnp.concatenate(pieces, axis=1)


def split_dot(values, matrix):
    high = lax.reduce_precision(values, exponent_bits=8, mantissa_bits=7)
    low = values - high
    return jnp.dot(
        high.astype(jnp.bfloat16), matrix, preferred_element_type=jnp.float32
    ) + jnp.dot(low.astype(jnp.bfloat16), matrix, preferred_element_type=jnp.float32)


def head_norm(attended):
    width = attended.shape[1]
    member = (jnp.arange(width)[:, None] // HEAD_DIM == jnp.arange(HEADS)[None, :]).astype(jnp.bfloat16)
    mean_square = split_dot(attended * attended, member) / HEAD_DIM
    scale = split_dot(lax.rsqrt(mean_square + epsilon), member.T)
    return attended * scale


def per_device(
    query_heads, key_heads, value_heads, head_gain, spatial_kernel, temporal_kernel, out_weight
):
    frame_count, row_count, col_count, model_width = query_heads.shape
    weight_cols = lax.all_gather(out_weight, "space", axis=0, tiled=True)
    weight_stack = lax.all_gather(weight_cols, "tm", axis=0)
    token_count = frame_count * row_count * col_count
    queries = query_heads.reshape(token_count, HEADS, HEAD_DIM)
    key_rows = key_heads.reshape(token_count, HEADS, HEAD_DIM)
    value_rows = value_heads.reshape(token_count, HEADS, HEAD_DIM)
    local_state = jnp.einsum(
        "thd,the->hde", jnp.maximum(key_rows, 0), value_rows, preferred_element_type=jnp.float32
    )
    padded = extended(value_heads, (("space", 1),), 1)
    spatial = spatial_conv(padded, spatial_kernel)
    earlier_frames = from_behind(spatial, "tm", 1)
    weight_flat = weight_stack.transpose(1, 0, 2).reshape(model_width, model_width)
    state_low, spatial, weight_flat = prefix_state(local_state, spatial, weight_flat)
    flat_queries = jnp.maximum(query_heads.reshape(token_count, model_width), 0)
    attended = banded_attention(flat_queries, state_low)
    normed = head_norm(attended).reshape(frame_count, row_count, col_count, model_width) * head_gain
    window = jnp.concatenate([earlier_frames, spatial], axis=0)
    temporal = jnp.zeros(normed.shape, jnp.float32)
    for back_step in range(3):
        temporal = temporal + temporal_kernel[back_step] * window[
            2 - back_step : 2 - back_step + frame_count
        ].astype(jnp.float32)
    mixed = (normed + temporal).astype(jnp.bfloat16).reshape(token_count, model_width)
    projected = jnp.dot(
        mixed, weight_flat, preferred_element_type=jnp.float32
    )
    return projected.astype(jnp.bfloat16).reshape(frame_count, row_count, col_count, model_width)


def solution(mesh):
    placed = (
        P("tm", "space", None, None),
        P("tm", "space", None, None),
        P("tm", "space", None, None),
        P(),
        P(),
        P(),
        P("space", "tm"),
    )
    return jax.shard_map(
        per_device,
        mesh=mesh,
        in_specs=placed,
        out_specs=P("tm", "space", None, None),
        check_vma=False,
    )
```

```python
import math

import jax
import jax.numpy as jnp
from jax import lax
from jax.sharding import PartitionSpec as P

HEADS = 20
HEAD_DIM = 112


epsilon = 1e-06


def extended(block, sides, width):
    for axis, dim in sides:
        count = lax.axis_size(axis)
        forward = [(i, i + 1) for i in range(count - 1)]
        backward = [(target, source) for source, target in forward]
        low = lax.ppermute(
            lax.slice_in_dim(block, block.shape[dim] - width, None, axis=dim), axis, forward
        )
        high = lax.ppermute(lax.slice_in_dim(block, 0, width, axis=dim), axis, backward)
        block = jnp.concatenate([low, block, high], axis=dim)
    return block


def from_behind(block, axis, distance):
    devices = range(lax.axis_size(axis))
    route = [(i - distance, i) for i in devices if i - distance in devices]
    return lax.ppermute(block, axis, route)


def prefix_state(local_state, beside_out, beside_back):
    axes = ("tm", "space")
    blocks, bands = lax.axis_size("tm"), lax.axis_size("space")
    devices = blocks * bands
    flat = local_state.reshape(devices, -1)
    chunk = flat.shape[1]
    mine = lax.all_to_all(flat, axes, 0, 0, tiled=True)
    mine, beside_out = lax.optimization_barrier((mine, beside_out))
    block_sums = mine.reshape(blocks, bands, chunk).sum(axis=1)
    prefixes = jnp.cumsum(block_sums, axis=0).astype(jnp.bfloat16)
    outgoing = jnp.broadcast_to(prefixes[:, None, :], (blocks, bands, chunk)).reshape(devices, chunk)
    gathered = lax.all_to_all(outgoing, axes, 0, 0, tiled=True)
    gathered, beside_back = lax.optimization_barrier((gathered, beside_back))
    return gathered.reshape(local_state.shape), beside_out, beside_back


def spatial_conv(padded, spatial_kernel):
    frame_count = padded.shape[0]
    row_count = padded.shape[1] - 2
    col_count = padded.shape[2]
    widened = jnp.pad(padded, ((0, 0), (0, 0), (1, 1), (0, 0)))
    summed = jnp.zeros((frame_count, row_count, col_count, padded.shape[3]), jnp.float32)
    for row_step in range(3):
        for col_step in range(3):
            summed = summed + spatial_kernel[3 * row_step + col_step] * widened[
                :, row_step : row_step + row_count, col_step : col_step + col_count
            ].astype(jnp.float32)
    return summed.astype(jnp.bfloat16)


def banded_attention(queries, state_low):
    heads, dim, _ = state_low.shape
    group = math.lcm(dim, 128) // dim
    pieces = []
    for first in range(0, heads, group):
        count = min(group, heads - first)
        blocks = state_low[first : first + count]
        eye = jnp.eye(count, dtype=bool)
        diagonal = jnp.where(
            eye[:, None, :, None], blocks[:, :, None, :], jnp.zeros((), blocks.dtype)
        ).reshape(count * dim, count * dim)
        pieces.append(
            jnp.dot(
                queries[:, first * dim : (first + count) * dim],
                diagonal,
                preferred_element_type=jnp.float32,
            )
        )
    return jnp.concatenate(pieces, axis=1)


def split_dot(values, matrix):
    high = lax.reduce_precision(values, exponent_bits=8, mantissa_bits=7)
    low = values - high
    return jnp.dot(
        high.astype(jnp.bfloat16), matrix, preferred_element_type=jnp.float32
    ) + jnp.dot(low.astype(jnp.bfloat16), matrix, preferred_element_type=jnp.float32)


def head_norm(attended):
    width = attended.shape[1]
    member = (jnp.arange(width)[:, None] // HEAD_DIM == jnp.arange(HEADS)[None, :]).astype(jnp.bfloat16)
    mean_square = split_dot(attended * attended, member) / HEAD_DIM
    scale = split_dot(lax.rsqrt(mean_square + epsilon), member.T)
    return attended * scale


def per_device(
    query_heads, key_heads, value_heads, head_gain, spatial_kernel, temporal_kernel, out_weight
):
    frame_count, row_count, col_count, model_width = query_heads.shape
    weight_cols = lax.all_gather(out_weight, "space", axis=0, tiled=True)
    column_pad = -weight_cols.shape[1] % 16
    weight_stack = lax.all_gather(jnp.pad(weight_cols, ((0, 0), (0, column_pad))), "tm", axis=0)
    token_count = frame_count * row_count * col_count
    queries = query_heads.reshape(token_count, HEADS, HEAD_DIM)
    key_rows = key_heads.reshape(token_count, HEADS, HEAD_DIM)
    value_rows = value_heads.reshape(token_count, HEADS, HEAD_DIM)
    local_state = jnp.einsum(
        "thd,the->hde", jnp.maximum(key_rows, 0), value_rows, preferred_element_type=jnp.float32
    )
    padded = extended(value_heads, (("space", 1),), 1)
    spatial = spatial_conv(padded, spatial_kernel)
    earlier_frames = from_behind(spatial, "tm", 1)
    blocks, _, padded_width = weight_stack.shape
    weight_flat = weight_stack.transpose(1, 0, 2).reshape(model_width, blocks * padded_width)
    state_low, spatial, (weight_flat, earlier_frames) = prefix_state(
        local_state, spatial, (weight_flat, earlier_frames)
    )
    flat_queries = jnp.maximum(query_heads.reshape(token_count, model_width), 0)
    attended = banded_attention(flat_queries, state_low)
    normed = head_norm(attended).reshape(frame_count, row_count, col_count, model_width) * head_gain
    window = jnp.concatenate([earlier_frames, spatial], axis=0)
    temporal = jnp.zeros(normed.shape, jnp.float32)
    for back_step in range(3):
        temporal = temporal + temporal_kernel[back_step] * window[
            2 - back_step : 2 - back_step + frame_count
        ].astype(jnp.float32)
    mixed = (normed + temporal).astype(jnp.bfloat16).reshape(token_count, model_width)
    projected = jnp.dot(mixed, weight_flat, preferred_element_type=jnp.float32)
    projected = projected.reshape(token_count, blocks, padded_width)[:, :, : padded_width - column_pad]
    return projected.astype(jnp.bfloat16).reshape(frame_count, row_count, col_count, model_width)


def solution(mesh):
    placed = (
        P("tm", "space", None, None),
        P("tm", "space", None, None),
        P("tm", "space", None, None),
        P(),
        P(),
        P(),
        P("space", "tm"),
    )
    return jax.shard_map(
        per_device,
        mesh=mesh,
        in_specs=placed,
        out_specs=P("tm", "space", None, None),
        check_vma=False,
    )
```

```python
import math

import jax
import jax.numpy as jnp
from jax import lax
from jax.sharding import PartitionSpec as P

HEADS = 20
HEAD_DIM = 112


epsilon = 1e-06


def extended(block, sides, width):
    for axis, dim in sides:
        count = lax.axis_size(axis)
        forward = [(i, i + 1) for i in range(count - 1)]
        backward = [(target, source) for source, target in forward]
        low = lax.ppermute(
            lax.slice_in_dim(block, block.shape[dim] - width, None, axis=dim), axis, forward
        )
        high = lax.ppermute(lax.slice_in_dim(block, 0, width, axis=dim), axis, backward)
        block = jnp.concatenate([low, block, high], axis=dim)
    return block


def from_behind(block, axis, distance):
    devices = range(lax.axis_size(axis))
    route = [(i - distance, i) for i in devices if i - distance in devices]
    return lax.ppermute(block, axis, route)


def prefix_state(local_state, beside_out, beside_back):
    axes = ("tm", "space")
    blocks, bands = lax.axis_size("tm"), lax.axis_size("space")
    devices = blocks * bands
    flat = local_state.reshape(devices, -1)
    chunk = flat.shape[1]
    mine = lax.all_to_all(flat, axes, 0, 0, tiled=True)
    mine, beside_out = lax.optimization_barrier((mine, beside_out))
    block_sums = mine.reshape(blocks, bands, chunk).sum(axis=1)
    prefixes = jnp.cumsum(block_sums, axis=0).astype(jnp.bfloat16)
    outgoing = jnp.broadcast_to(prefixes[:, None, :], (blocks, bands, chunk)).reshape(devices, chunk)
    gathered = lax.all_to_all(outgoing, axes, 0, 0, tiled=True)
    gathered, beside_back = lax.optimization_barrier((gathered, beside_back))
    return gathered.reshape(local_state.shape), beside_out, beside_back


def spatial_conv(padded, spatial_kernel):
    frame_count = padded.shape[0]
    row_count = padded.shape[1] - 2
    col_count = padded.shape[2]
    widened = jnp.pad(padded, ((0, 0), (0, 0), (1, 1), (0, 0)))
    summed = jnp.zeros((frame_count, row_count, col_count, padded.shape[3]), jnp.float32)
    for row_step in range(3):
        for col_step in range(3):
            summed = summed + spatial_kernel[3 * row_step + col_step] * widened[
                :, row_step : row_step + row_count, col_step : col_step + col_count
            ].astype(jnp.float32)
    return summed.astype(jnp.bfloat16)


def banded_state(keys, values):
    group = math.lcm(HEAD_DIM, 128) // HEAD_DIM
    blocks = []
    for first in range(0, HEADS, group):
        count = min(group, HEADS - first)
        span = slice(first * HEAD_DIM, (first + count) * HEAD_DIM)
        product = lax.dot_general(
            keys[:, span], values[:, span], (((0,), (0,)), ((), ())), preferred_element_type=jnp.float32
        )
        for head in range(count):
            rows = slice(head * HEAD_DIM, (head + 1) * HEAD_DIM)
            blocks.append(product[rows, rows])
    return jnp.stack(blocks)


def banded_attention(queries, state_low):
    heads, dim, _ = state_low.shape
    group = math.lcm(dim, 128) // dim
    pieces = []
    for first in range(0, heads, group):
        count = min(group, heads - first)
        blocks = state_low[first : first + count]
        eye = jnp.eye(count, dtype=bool)
        diagonal = jnp.where(
            eye[:, None, :, None], blocks[:, :, None, :], jnp.zeros((), blocks.dtype)
        ).reshape(count * dim, count * dim)
        pieces.append(
            jnp.dot(
                queries[:, first * dim : (first + count) * dim],
                diagonal,
                preferred_element_type=jnp.float32,
            )
        )
    return jnp.concatenate(pieces, axis=1)


def split_dot(values, matrix):
    high = lax.reduce_precision(values, exponent_bits=8, mantissa_bits=7)
    low = values - high
    return jnp.dot(
        high.astype(jnp.bfloat16), matrix, preferred_element_type=jnp.float32
    ) + jnp.dot(low.astype(jnp.bfloat16), matrix, preferred_element_type=jnp.float32)


def head_norm(attended):
    width = attended.shape[1]
    member = (jnp.arange(width)[:, None] // HEAD_DIM == jnp.arange(HEADS)[None, :]).astype(jnp.bfloat16)
    mean_square = split_dot(attended * attended, member) / HEAD_DIM
    scale = split_dot(lax.rsqrt(mean_square + epsilon), member.T)
    return attended * scale


def per_device(
    query_heads, key_heads, value_heads, head_gain, spatial_kernel, temporal_kernel, out_weight
):
    frame_count, row_count, col_count, model_width = query_heads.shape
    weight_cols = lax.all_gather(out_weight, "space", axis=0, tiled=True)
    weight_stack = lax.all_gather(weight_cols, "tm", axis=0)
    token_count = frame_count * row_count * col_count
    queries = query_heads.reshape(token_count, HEADS, HEAD_DIM)
    key_rows = key_heads.reshape(token_count, HEADS, HEAD_DIM)
    value_rows = value_heads.reshape(token_count, HEADS, HEAD_DIM)
    local_state = banded_state(
        jnp.maximum(key_heads.reshape(token_count, model_width), 0),
        value_heads.reshape(token_count, model_width),
    )
    padded = extended(value_heads, (("space", 1),), 1)
    spatial = spatial_conv(padded, spatial_kernel)
    earlier_frames = from_behind(spatial, "tm", 1)
    weight_flat = weight_stack.transpose(1, 0, 2).reshape(model_width, model_width)
    state_low, spatial, weight_flat = prefix_state(local_state, spatial, weight_flat)
    flat_queries = jnp.maximum(query_heads.reshape(token_count, model_width), 0)
    attended = banded_attention(flat_queries, state_low)
    normed = head_norm(attended).reshape(frame_count, row_count, col_count, model_width) * head_gain
    window = jnp.concatenate([earlier_frames, spatial], axis=0)
    temporal = jnp.zeros(normed.shape, jnp.float32)
    for back_step in range(3):
        temporal = temporal + temporal_kernel[back_step] * window[
            2 - back_step : 2 - back_step + frame_count
        ].astype(jnp.float32)
    mixed = (normed + temporal).astype(jnp.bfloat16).reshape(token_count, model_width)
    projected = jnp.dot(
        mixed, weight_flat, preferred_element_type=jnp.float32
    )
    return projected.astype(jnp.bfloat16).reshape(frame_count, row_count, col_count, model_width)


def solution(mesh):
    placed = (
        P("tm", "space", None, None),
        P("tm", "space", None, None),
        P("tm", "space", None, None),
        P(),
        P(),
        P(),
        P("space", "tm"),
    )
    return jax.shard_map(
        per_device,
        mesh=mesh,
        in_specs=placed,
        out_specs=P("tm", "space", None, None),
        check_vma=False,
    )
```

```python
import math

import jax
import jax.numpy as jnp
from jax import lax
from jax.sharding import PartitionSpec as P

HEADS = 20
HEAD_DIM = 112


epsilon = 1e-06


def extended(block, sides, width):
    for axis, dim in sides:
        count = lax.axis_size(axis)
        forward = [(i, i + 1) for i in range(count - 1)]
        backward = [(target, source) for source, target in forward]
        low = lax.ppermute(
            lax.slice_in_dim(block, block.shape[dim] - width, None, axis=dim), axis, forward
        )
        high = lax.ppermute(lax.slice_in_dim(block, 0, width, axis=dim), axis, backward)
        block = jnp.concatenate([low, block, high], axis=dim)
    return block


def from_behind(block, axis, distance):
    devices = range(lax.axis_size(axis))
    route = [(i - distance, i) for i in devices if i - distance in devices]
    return lax.ppermute(block, axis, route)


def prefix_state(local_state, beside_out, beside_back):
    axes = ("tm", "space")
    blocks, bands = lax.axis_size("tm"), lax.axis_size("space")
    devices = blocks * bands
    flat = local_state.reshape(devices, -1)
    chunk = flat.shape[1]
    mine = lax.all_to_all(flat, axes, 0, 0, tiled=True)
    mine, beside_out = lax.optimization_barrier((mine, beside_out))
    block_sums = mine.reshape(blocks, bands, chunk).sum(axis=1)
    prefixes = jnp.cumsum(block_sums, axis=0).astype(jnp.bfloat16)
    outgoing = jnp.broadcast_to(prefixes[:, None, :], (blocks, bands, chunk)).reshape(devices, chunk)
    gathered = lax.all_to_all(outgoing, axes, 0, 0, tiled=True)
    gathered, beside_back = lax.optimization_barrier((gathered, beside_back))
    return gathered.reshape(local_state.shape), beside_out, beside_back


def spatial_conv(padded, spatial_kernel):
    frame_count = padded.shape[0]
    row_count = padded.shape[1] - 2
    col_count = padded.shape[2]
    widened = jnp.pad(padded, ((0, 0), (0, 0), (1, 1), (0, 0)))
    summed = jnp.zeros((frame_count, row_count, col_count, padded.shape[3]), jnp.float32)
    for row_step in range(3):
        for col_step in range(3):
            summed = summed + spatial_kernel[3 * row_step + col_step] * widened[
                :, row_step : row_step + row_count, col_step : col_step + col_count
            ].astype(jnp.float32)
    return summed.astype(jnp.bfloat16)


def banded_state(keys, values):
    group = math.lcm(HEAD_DIM, 128) // HEAD_DIM
    blocks = []
    for first in range(0, HEADS, group):
        count = min(group, HEADS - first)
        span = slice(first * HEAD_DIM, (first + count) * HEAD_DIM)
        product = lax.dot_general(
            keys[:, span], values[:, span], (((0,), (0,)), ((), ())), preferred_element_type=jnp.float32
        )
        for head in range(count):
            rows = slice(head * HEAD_DIM, (head + 1) * HEAD_DIM)
            blocks.append(product[rows, rows])
    return jnp.stack(blocks)


def banded_attention(queries, state_low):
    heads, dim, _ = state_low.shape
    group = math.lcm(dim, 128) // dim
    pieces = []
    for first in range(0, heads, group):
        count = min(group, heads - first)
        blocks = state_low[first : first + count]
        eye = jnp.eye(count, dtype=bool)
        diagonal = jnp.where(
            eye[:, None, :, None], blocks[:, :, None, :], jnp.zeros((), blocks.dtype)
        ).reshape(count * dim, count * dim)
        pieces.append(
            jnp.dot(
                queries[:, first * dim : (first + count) * dim],
                diagonal,
                preferred_element_type=jnp.float32,
            )
        )
    return jnp.concatenate(pieces, axis=1)


def split_dot(values, matrix):
    high = lax.reduce_precision(values, exponent_bits=8, mantissa_bits=7)
    low = values - high
    return jnp.dot(
        high.astype(jnp.bfloat16), matrix, preferred_element_type=jnp.float32
    ) + jnp.dot(low.astype(jnp.bfloat16), matrix, preferred_element_type=jnp.float32)


def head_norm(attended):
    width = attended.shape[1]
    member = (jnp.arange(width)[:, None] // HEAD_DIM == jnp.arange(HEADS)[None, :]).astype(jnp.bfloat16)
    mean_square = split_dot(attended * attended, member) / HEAD_DIM
    scale = split_dot(lax.rsqrt(mean_square + epsilon), member.T)
    return attended * scale


def per_device(
    query_heads, key_heads, value_heads, head_gain, spatial_kernel, temporal_kernel, out_weight
):
    frame_count, row_count, col_count, model_width = query_heads.shape
    weight_band = lax.all_gather(out_weight, "tm", axis=1, tiled=True)
    weight_stack = lax.all_gather(weight_band, "space", axis=0)
    token_count = frame_count * row_count * col_count
    queries = query_heads.reshape(token_count, HEADS, HEAD_DIM)
    key_rows = key_heads.reshape(token_count, HEADS, HEAD_DIM)
    value_rows = value_heads.reshape(token_count, HEADS, HEAD_DIM)
    local_state = banded_state(
        jnp.maximum(key_heads.reshape(token_count, model_width), 0),
        value_heads.reshape(token_count, model_width),
    )
    padded = extended(value_heads, (("space", 1),), 1)
    spatial = spatial_conv(padded, spatial_kernel)
    earlier_frames = from_behind(spatial, "tm", 1)
    weight_flat = weight_stack.reshape(model_width, model_width)
    state_low, spatial, weight_flat = prefix_state(local_state, spatial, weight_flat)
    flat_queries = jnp.maximum(query_heads.reshape(token_count, model_width), 0)
    attended = banded_attention(flat_queries, state_low)
    normed = head_norm(attended).reshape(frame_count, row_count, col_count, model_width) * head_gain
    window = jnp.concatenate([earlier_frames, spatial], axis=0)
    temporal = jnp.zeros(normed.shape, jnp.float32)
    for back_step in range(3):
        temporal = temporal + temporal_kernel[back_step] * window[
            2 - back_step : 2 - back_step + frame_count
        ].astype(jnp.float32)
    mixed = (normed + temporal).astype(jnp.bfloat16).reshape(token_count, model_width)
    projected = jnp.dot(
        mixed, weight_flat, preferred_element_type=jnp.float32
    )
    return projected.astype(jnp.bfloat16).reshape(frame_count, row_count, col_count, model_width)


def solution(mesh):
    placed = (
        P("tm", "space", None, None),
        P("tm", "space", None, None),
        P("tm", "space", None, None),
        P(),
        P(),
        P(),
        P("space", "tm"),
    )
    return jax.shard_map(
        per_device,
        mesh=mesh,
        in_specs=placed,
        out_specs=P("tm", "space", None, None),
        check_vma=False,
    )
```

```python
import math

import jax
import jax.numpy as jnp
from jax import lax
from jax.sharding import PartitionSpec as P

HEADS = 20
HEAD_DIM = 112


epsilon = 1e-06


def extended(block, sides, width):
    for axis, dim in sides:
        count = lax.axis_size(axis)
        forward = [(i, i + 1) for i in range(count - 1)]
        backward = [(target, source) for source, target in forward]
        low = lax.ppermute(
            lax.slice_in_dim(block, block.shape[dim] - width, None, axis=dim), axis, forward
        )
        high = lax.ppermute(lax.slice_in_dim(block, 0, width, axis=dim), axis, backward)
        block = jnp.concatenate([low, block, high], axis=dim)
    return block


def from_behind(block, axis, distance):
    devices = range(lax.axis_size(axis))
    route = [(i - distance, i) for i in devices if i - distance in devices]
    return lax.ppermute(block, axis, route)


def prefix_state(local_state, beside_out, beside_back):
    axes = ("tm", "space")
    blocks, bands = lax.axis_size("tm"), lax.axis_size("space")
    devices = blocks * bands
    flat = local_state.reshape(devices, -1)
    chunk = flat.shape[1]
    mine = lax.all_to_all(flat, axes, 0, 0, tiled=True)
    mine, beside_out = lax.optimization_barrier((mine, beside_out))
    block_sums = mine.reshape(blocks, bands, chunk).sum(axis=1)
    prefixes = jnp.cumsum(block_sums, axis=0).astype(jnp.bfloat16)
    outgoing = jnp.broadcast_to(prefixes[:, None, :], (blocks, bands, chunk)).reshape(devices, chunk)
    gathered = lax.all_to_all(outgoing, axes, 0, 0, tiled=True)
    gathered, beside_back = lax.optimization_barrier((gathered, beside_back))
    return gathered.reshape(local_state.shape), beside_out, beside_back


def spatial_conv(padded, spatial_kernel):
    frame_count = padded.shape[0]
    row_count = padded.shape[1] - 2
    col_count = padded.shape[2]
    widened = jnp.pad(padded, ((0, 0), (0, 0), (1, 1), (0, 0)))
    summed = jnp.zeros((frame_count, row_count, col_count, padded.shape[3]), jnp.float32)
    for row_step in range(3):
        for col_step in range(3):
            summed = summed + spatial_kernel[3 * row_step + col_step] * widened[
                :, row_step : row_step + row_count, col_step : col_step + col_count
            ].astype(jnp.float32)
    return summed.astype(jnp.bfloat16)


def banded_state(keys, values):
    group = math.lcm(HEAD_DIM, 128) // HEAD_DIM
    blocks = []
    for first in range(0, HEADS, group):
        count = min(group, HEADS - first)
        span = slice(first * HEAD_DIM, (first + count) * HEAD_DIM)
        product = lax.dot_general(
            keys[:, span], values[:, span], (((0,), (0,)), ((), ())), preferred_element_type=jnp.float32
        )
        for head in range(count):
            rows = slice(head * HEAD_DIM, (head + 1) * HEAD_DIM)
            blocks.append(product[rows, rows])
    return jnp.stack(blocks)


def banded_attention(queries, state_low):
    heads, dim, _ = state_low.shape
    group = math.lcm(dim, 128) // dim
    pieces = []
    for first in range(0, heads, group):
        count = min(group, heads - first)
        blocks = state_low[first : first + count]
        eye = jnp.eye(count, dtype=bool)
        diagonal = jnp.where(
            eye[:, None, :, None], blocks[:, :, None, :], jnp.zeros((), blocks.dtype)
        ).reshape(count * dim, count * dim)
        pieces.append(
            jnp.dot(
                queries[:, first * dim : (first + count) * dim],
                diagonal,
                preferred_element_type=jnp.float32,
            )
        )
    return jnp.concatenate(pieces, axis=1)


def split_dot(values, matrix):
    high = lax.reduce_precision(values, exponent_bits=8, mantissa_bits=7)
    low = values - high
    return jnp.dot(
        high.astype(jnp.bfloat16), matrix, preferred_element_type=jnp.float32
    ) + jnp.dot(low.astype(jnp.bfloat16), matrix, preferred_element_type=jnp.float32)


def head_norm(attended):
    width = attended.shape[1]
    member = (jnp.arange(width)[:, None] // HEAD_DIM == jnp.arange(HEADS)[None, :]).astype(jnp.bfloat16)
    mean_square = split_dot(attended * attended, member) / HEAD_DIM
    scale = split_dot(lax.rsqrt(mean_square + epsilon), member.T)
    return attended * scale


def per_device(
    query_heads, key_heads, value_heads, head_gain, spatial_kernel, temporal_kernel, out_weight
):
    frame_count, row_count, col_count, model_width = query_heads.shape
    weight_cols = lax.all_gather(out_weight, "space", axis=0, tiled=True)
    weight_stack = lax.all_gather(weight_cols, "tm", axis=0)
    token_count = frame_count * row_count * col_count
    queries = query_heads.reshape(token_count, HEADS, HEAD_DIM)
    key_rows = key_heads.reshape(token_count, HEADS, HEAD_DIM)
    value_rows = value_heads.reshape(token_count, HEADS, HEAD_DIM)
    local_state = banded_state(
        jnp.maximum(key_heads.reshape(token_count, model_width), 0),
        value_heads.reshape(token_count, model_width),
    )
    padded = extended(value_heads, (("space", 1),), 1)
    spatial = spatial_conv(padded, spatial_kernel)
    earlier_frames = from_behind(spatial, "tm", 1)
    state_low, spatial, _ = prefix_state(local_state, spatial, ())
    flat_queries = jnp.maximum(query_heads.reshape(token_count, model_width), 0)
    attended = banded_attention(flat_queries, state_low)
    attended, weight_stack = lax.optimization_barrier((attended, weight_stack))
    weight_flat = weight_stack.transpose(1, 0, 2).reshape(model_width, model_width)
    normed = head_norm(attended).reshape(frame_count, row_count, col_count, model_width) * head_gain
    window = jnp.concatenate([earlier_frames, spatial], axis=0)
    temporal = jnp.zeros(normed.shape, jnp.float32)
    for back_step in range(3):
        temporal = temporal + temporal_kernel[back_step] * window[
            2 - back_step : 2 - back_step + frame_count
        ].astype(jnp.float32)
    mixed = (normed + temporal).astype(jnp.bfloat16).reshape(token_count, model_width)
    projected = jnp.dot(
        mixed, weight_flat, preferred_element_type=jnp.float32
    )
    return projected.astype(jnp.bfloat16).reshape(frame_count, row_count, col_count, model_width)


def solution(mesh):
    placed = (
        P("tm", "space", None, None),
        P("tm", "space", None, None),
        P("tm", "space", None, None),
        P(),
        P(),
        P(),
        P("space", "tm"),
    )
    return jax.shard_map(
        per_device,
        mesh=mesh,
        in_specs=placed,
        out_specs=P("tm", "space", None, None),
        check_vma=False,
    )
```
